256 devices in a mesh: req: 32 (over y, z), head: 8 (over x, core).
Axes of the slice: x: 4, y: 4, z: 8, core: 2. Of those that a mesh axis runs over, the one named last changes fastest.
Arguments:
- tokens: bfloat16 [32768, 1024], P(('req', 'head')), may hold values from -6 to 6
- w_proj: bfloat16 [1024, 2048], P(None, 'head'), may hold values from -0.1875 to 0.1875
- w_out: bfloat16 [1024, 1024], replicated, may hold values from -0.1875 to 0.1875
- kv_cache: bfloat16 [32, 32, 3, 128, 2048], P('req', None, None, None, 'head'), may hold values from -6 to 6
- slot_request: int32 [64], P('req'), may hold values from 0 to 63, each once
- lengths: int32 [64], replicated, may hold values from 1 to 4096
- block_owner: int32 [2048, 1], P('req'), may hold values from 0 to 31; in each aligned block of 64 rows (0 to 63, 64 to 127, ...) at most 3 rows name the same one
Outputs:
- mixed: bfloat16 [32768, 1024], P(('req', 'head'))
The draws below stay inside these ranges and needn't reach their ends.
Inputs may be any that keep to these rules, and one draw needn't show every extreme that they name: `block_owner`: within each aligned block of 64 rows no owner appears more than 3 times.
All inputs are finite; a program needn't handle non-finite values.
Results may differ from the reference program's by a relative error of at most 0.0088.
Values may be sent and summed in bfloat16 or wider, within the bound.
No kernel may reach another device: no remote copies, remote signals or barrier semaphores. Data moves between devices by JAX's collectives and lax.ppermute only.
A program may use at most 128 MiB of HBM per device.

```python
import math
import jax
import jax.numpy as jnp
import numpy as np
from jax import lax

D = 1024
H = 16
DH = 64
CAND = 512
BLK = 128
MAXB = 32
REQ_DEV = 2
HIST = 4096
REQS = 64
TOKENS = 32768
MOST = 3
N_REQ = 32


def draw_lengths(key, part):
    first, second = jax.random.split(key)
    values = jax.random.randint(first, (REQS,), 1, HIST + 1)
    spot = jax.random.randint(second, (), 0, REQS)
    places = jnp.arange(REQS)
    values = jnp.where(places == spot, HIST, values)
    values = jnp.where(places == (spot + 1) % REQS, 1, values)
    return values.astype(jnp.int32)


def block_levels(own_key, extent, cuts, low, high):
    level = 1.0
    for dim, blocks in cuts:
        draws = jax.random.uniform(jax.random.fold_in(jax.random.fold_in(own_key, 6), dim), (blocks,), jnp.float32, low / len(cuts), high / len(cuts))
        level = level * jnp.repeat(jnp.exp(draws), extent[dim] // blocks).reshape((-1,) + (1,) * (len(extent) - 1 - dim))
    return level


def assign_block(stream_key, own, number, rows, number_of, top, limit, slope):
    order = jax.random.permutation(stream_key, number_of)
    packed, common = shares(number_of, rows * top, limit, slope, True), shares(number_of, rows * top, limit, slope, False)
    places = jnp.arange(number_of)

    def named(sizes, offset_by):
        used = int((sizes > 0).sum())
        fixed = max(1, used // 4)
        moved = fixed + (places - fixed + offset_by * (used - fixed)) % max(1, number_of - fixed)
        return jnp.zeros((number_of,), jnp.int32).at[order[jnp.where(places < fixed, places, moved)]].set(jnp.asarray(sizes, jnp.int32))

    sizes = jnp.where(number % 4 == 0, named(packed, number // 4), named(common, number - number // 4 - 1))
    mixed = jax.random.permutation(jax.random.fold_in(own, 3), number_of)
    source_of, sink = mixed[0:number_of // 2 * 2:2], mixed[1:number_of // 2 * 2:2]
    room = jnp.minimum(sizes[source_of] - 1, limit - sizes[sink]) // 2
    room = jnp.where((source_of == order[0]) | (sink == order[0]) | (sizes[sink] == 0), 0, jnp.maximum(room, 0))
    moved = jax.random.randint(jax.random.fold_in(own, 4), (number_of // 2,), 0, 1 << 20) % (room + 1)
    sizes = sizes.at[source_of].add(-moved).at[sink].add(moved)
    members = jnp.searchsorted(jnp.cumsum(sizes), jnp.arange(rows * top), side="right").astype(jnp.int32)
    listing = members.reshape(top, rows).T
    listing = listing[jax.random.permutation(jax.random.fold_in(own, 1), rows)]
    offset_by = jax.random.randint(jax.random.fold_in(own, 2), (rows, 1), 0, top)
    return jnp.take_along_axis(listing, (jnp.arange(top)[None, :] + offset_by) % top, axis=1)


def shares(amount, total, most, slope, full):
    weights = [(1 << 20) // math.isqrt(rank ** slope) + 1 for rank in range(1, amount + 1)]
    largest = most if full else min(most, max(-(-total // amount), total * weights[0] // sum(weights)))
    least = 1 if total - largest >= amount - 1 else 0
    given, surplus = [largest] + [least] * (amount - 1), total - largest - least * (amount - 1)
    while surplus > 0:
        movable = [i for i in range(1, amount) if given[i] < largest] or [i for i in range(1, amount) if given[i] < most]
        mass, left = sum([weights[i] for i in movable]), surplus
        for i in movable:
            extra = min(most - given[i], max(1, left * weights[i] // mass), surplus)
            given[i] = given[i] + extra
            surplus = surplus - extra
    return np.array(given)


def gaussian(rng, extent, width, limit, shards=(), held_as=jnp.bfloat16):
    drawn = width * jax.random.normal(rng, extent, jnp.float32)
    if shards:
        drawn = drawn * block_levels(rng, extent, shards, -0.22, 0.18)
    return jnp.clip(drawn, -limit, limit).astype(held_as)


def setup_inputs(seed: int = 0) -> dict:
    streams_of = jax.random.split(jax.random.key(seed), 8)
    tokens = gaussian(streams_of[0], (TOKENS, D), 1.0, 6.0, ((0, 256),))
    w_proj = gaussian(streams_of[1], (D, H * 2 * DH), D ** -0.5, 0.1875, ((1, 8),))
    w_out = gaussian(streams_of[2], (H * DH, D), (H * DH) ** -0.5, 0.1875)
    kv_cache = gaussian(streams_of[3], (N_REQ, N_REQ, MOST, BLK, H * 2 * DH), 1.0, 6.0, ((0, 32), (4, 8)))
    slot_request = jax.random.permutation(streams_of[4], REQS).astype(jnp.int32)
    lengths = draw_lengths(jax.random.fold_in(streams_of[7], 71), 0)
    block_owner_keys = jax.random.split(jax.random.fold_in(streams_of[6], 1), (REQS * MAXB) // (REQ_DEV * MAXB))
    block_owner_turns = jax.random.permutation(jax.random.fold_in(streams_of[6], 3), (REQS * MAXB) // (REQ_DEV * MAXB))
    block_owner = jax.vmap(lambda own, number: assign_block(jax.random.fold_in(streams_of[6], 2), own, number, REQ_DEV * MAXB, N_REQ, 1, MOST, 2))(block_owner_keys, block_owner_turns).reshape((REQS * MAXB, 1))
    return dict(tokens=tokens, w_proj=w_proj, w_out=w_out, kv_cache=kv_cache, slot_request=slot_request, lengths=lengths, block_owner=block_owner)


def layer_norm(values):
    mean = lax.optimization_barrier(jnp.mean(values, axis=-1, keepdims=True))
    square = lax.optimization_barrier(jnp.mean(values * values, axis=-1, keepdims=True))
    return (values - mean) * lax.rsqrt(square - mean * mean + 1e-05)

def reference(tokens, w_proj, w_out, kv_cache, slot_request, lengths, block_owner):
    normed = layer_norm(tokens.astype(jnp.float32)).astype(jnp.bfloat16)
    proj = jax.nn.silu(jnp.dot(normed, w_proj, preferred_element_type=jnp.float32))
    proj = proj.reshape(TOKENS, H, 2, DH)
    gate_u = proj[:, :, 0].astype(jnp.bfloat16)
    query = proj[:, :, 1].astype(jnp.bfloat16)
    lens = lengths[slot_request].reshape(N_REQ, REQ_DEV)
    owners = block_owner[:, 0].astype(jnp.int32).reshape(N_REQ, REQ_DEV * MAXB)
    onehot = (owners[:, :, None] == jnp.arange(N_REQ, dtype=jnp.int32)[None, None, :]).astype(jnp.int32)
    rank = lax.optimization_barrier(jnp.sum((jnp.cumsum(onehot, axis=1) - onehot) * onehot, axis=2))
    index = (owners * MOST + rank).astype(jnp.int32)
    query_dev = query.reshape(N_REQ, REQ_DEV, CAND, H, DH)
    scale = 1.0 / DH ** 0.5
    positions = jnp.arange(HIST, dtype=jnp.int32)

    def per_scorer(scorer):
        pool = kv_cache[:, scorer].reshape(N_REQ * MOST, BLK, H * 2 * DH)
        history = pool[index[scorer]].reshape(REQ_DEV, HIST, H, 2, DH)

        def per_request(slot):
            keys = history[slot, :, :, 0].astype(jnp.float32)
            values = history[slot, :, :, 1].astype(jnp.float32)
            scores = jnp.einsum('chd,phd->hcp', query_dev[scorer, slot].astype(jnp.float32), keys) * scale
            live = positions < lens[scorer, slot]
            weights = jnp.where(live[None, None, :], jax.nn.silu(scores), 0.0).astype(jnp.bfloat16)
            weights = lax.optimization_barrier(weights).astype(jnp.float32)
            return jnp.einsum('hcp,phd->chd', weights, values)
        return lax.map(per_request, jnp.arange(REQ_DEV, dtype=jnp.int32))
    attn = lax.map(per_scorer, jnp.arange(N_REQ, dtype=jnp.int32))
    attn = attn.reshape(TOKENS, H * DH).astype(jnp.bfloat16)
    hidden = layer_norm(attn.astype(jnp.float32)) * gate_u.reshape(TOKENS, H * DH).astype(jnp.float32)
    hidden = hidden.astype(jnp.bfloat16)
    return jnp.dot(hidden, w_out, preferred_element_type=jnp.float32).astype(jnp.bfloat16)
```

```python
import functools

import jax
import jax.numpy as jnp
from jax import lax
from jax.experimental import pallas as pl
from jax.experimental.pallas import tpu as pltpu
from jax.sharding import PartitionSpec as P

DH = 64
CAND = 512
BLK = 128
MAXB = 32


def layer_norm(values):
    mean = jnp.mean(values, axis=-1, keepdims=True)
    square = jnp.mean(values * values, axis=-1, keepdims=True)
    return (values - mean) * lax.rsqrt(square - mean * mean + 1e-05)


def attention_kernel(index_ref, length_ref, query_ref, pool_ref, out_ref, acc_ref, *, heads):
    slot = pl.program_id(0)
    block = pl.program_id(1)
    length = length_ref[slot]

    @pl.when(block == 0)
    def _():
        acc_ref[...] = jnp.zeros_like(acc_ref)

    @pl.when(block * BLK < length)
    def _():
        kv = pool_ref[0]
        positions = block * BLK + lax.broadcasted_iota(jnp.int32, (1, BLK), 1)
        live = positions < length
        for h in range(heads):
            lanes = slice(h * 2 * DH, (h + 1) * 2 * DH)
            pair = kv[:, lanes]
            query = query_ref[:, lanes]
            scores = lax.dot_general(
                query, pair, (((1,), (1,)), ((), ())), preferred_element_type=jnp.float32
            ) * (1.0 / DH**0.5)
            weights = scores / (1.0 + jnp.exp(-scores))
            weights = jnp.where(live, weights, 0.0).astype(jnp.bfloat16)
            acc_ref[:, lanes] += jnp.dot(weights, pair, preferred_element_type=jnp.float32)

    @pl.when(block == pl.num_programs(1) - 1)
    def _():
        out_ref[...] = acc_ref[...].astype(out_ref.dtype)


def attention(index, slot_lengths, query_pad, pool):
    rows, width = query_pad.shape
    slots = rows // CAND
    heads = width // (2 * DH)
    kernel = functools.partial(attention_kernel, heads=heads)
    grid_spec = pltpu.PrefetchScalarGridSpec(
        num_scalar_prefetch=2,
        grid=(slots, MAXB),
        in_specs=[
            pl.BlockSpec((CAND, width), lambda s, j, idx, lens: (s, 0)),
            pl.BlockSpec((1, BLK, width), lambda s, j, idx, lens: (idx[s * MAXB + j], 0, 0)),
        ],
        out_specs=pl.BlockSpec((CAND, width), lambda s, j, idx, lens: (s, 0)),
        scratch_shapes=[pltpu.VMEM((CAND, width), jnp.float32)],
    )
    return pl.pallas_call(
        kernel,
        grid_spec=grid_spec,
        out_shape=jax.ShapeDtypeStruct((rows, width), jnp.bfloat16),
        compiler_params=pltpu.CompilerParams(dimension_semantics=("arbitrary", "arbitrary")),
    )(index, slot_lengths, query_pad, pool)


def shards(tokens, w_proj, w_out, kv_cache, slot_request, lengths, block_owner):
    head_local = w_proj.shape[1] // (2 * DH)
    received = lax.all_to_all(kv_cache, "req", split_axis=1, concat_axis=0, tiled=True)
    most_slots = received.shape[2]
    pool = received.reshape(-1, BLK, received.shape[-1])
    pool_count = pool.shape[0]

    gathered = lax.all_gather(tokens, "head", axis=0, tiled=True)
    normed = layer_norm(gathered.astype(jnp.float32)).astype(jnp.bfloat16)
    row_count = normed.shape[0]
    slots = row_count // CAND
    proj = jax.nn.silu(jnp.dot(normed, w_proj, preferred_element_type=jnp.float32))
    proj = proj.reshape(row_count, head_local, 2, DH)
    gate_u = proj[:, :, 0].astype(jnp.bfloat16).reshape(row_count, head_local * DH)
    query = proj[:, :, 1].astype(jnp.bfloat16)
    query_pad = jnp.concatenate([query, jnp.zeros_like(query)], axis=2).reshape(
        row_count, head_local * 2 * DH
    )

    owner_count = lax.axis_size("req")
    owners = block_owner[:, 0]
    onehot = (owners[:, None] == jnp.arange(owner_count, dtype=jnp.int32)[None, :]).astype(
        jnp.int32
    )
    rank = jnp.sum((jnp.cumsum(onehot, axis=0) - onehot) * onehot, axis=1)
    index = jnp.clip(owners * most_slots + rank, 0, pool_count - 1).reshape(slots, MAXB)
    total_requests = lengths.shape[0]
    match = slot_request[:, None] == jnp.arange(total_requests, dtype=jnp.int32)[None, :]
    slot_lengths = jnp.sum(jnp.where(match, lengths[None, :], 0), axis=1).astype(jnp.int32)
    last_live = jnp.clip((slot_lengths - 1) // BLK, 0, MAXB - 1)
    blocks = jnp.minimum(jnp.arange(MAXB, dtype=jnp.int32)[None, :], last_live[:, None])
    index = jnp.take_along_axis(index, blocks, axis=1).reshape(-1).astype(jnp.int32)

    out = attention(index, slot_lengths, query_pad, pool)
    attn = out.reshape(row_count, head_local, 2, DH)[:, :, 1].reshape(row_count, head_local * DH)

    mixed_in = jnp.stack([attn, gate_u])
    moved = lax.all_to_all(mixed_in, "head", split_axis=1, concat_axis=2, tiled=True)
    attn_rows = moved[0].astype(jnp.float32)
    gate_rows = moved[1].astype(jnp.float32)
    hidden = (layer_norm(attn_rows) * gate_rows).astype(jnp.bfloat16)
    return jnp.dot(hidden, w_out, preferred_element_type=jnp.float32).astype(jnp.bfloat16)


def solution(mesh):
    return jax.shard_map(
        shards,
        mesh=mesh,
        in_specs=(
            P(("req", "head"), None),
            P(None, "head"),
            P(),
            P("req", None, None, None, "head"),
            P("req"),
            P(),
            P("req", None),
        ),
        out_specs=P(("req", "head"), None),
        check_vma=False,
    )
```

```python
import functools

import jax
import jax.numpy as jnp
from jax import lax
from jax.experimental import pallas as pl
from jax.experimental.pallas import tpu as pltpu
from jax.sharding import PartitionSpec as P

DH = 64
CAND = 512
BLK = 128
MAXB = 32


def layer_norm(values):
    mean = jnp.mean(values, axis=-1, keepdims=True)
    square = jnp.mean(values * values, axis=-1, keepdims=True)
    return (values - mean) * lax.rsqrt(square - mean * mean + 1e-05)


def attention_kernel(index_ref, length_ref, query_ref, *refs, heads, group):
    pool_refs = refs[:group]
    out_ref, acc_ref = refs[group:]
    slot = pl.program_id(0)
    step = pl.program_id(1)
    length = length_ref[slot]

    @pl.when(step == 0)
    def _():
        acc_ref[...] = jnp.zeros_like(acc_ref)

    for i in range(group):
        block = step * group + i

        @pl.when(block * BLK < length)
        def _():
            kv = pool_refs[i][0]
            positions = block * BLK + lax.broadcasted_iota(jnp.int32, (1, BLK), 1)
            live = positions < length
            for h in range(heads):
                lanes = slice(h * 2 * DH, (h + 1) * 2 * DH)
                pair = kv[:, lanes]
                query = query_ref[:, lanes]
                half = lax.dot_general(
                    query, pair, (((1,), (1,)), ((), ())), preferred_element_type=jnp.float32
                ) * (0.5 / DH**0.5)
                weights = half + half * jnp.tanh(half)
                weights = jnp.where(live, weights, 0.0).astype(jnp.bfloat16)
                acc_ref[:, lanes] += jnp.dot(weights, pair, preferred_element_type=jnp.float32)

    @pl.when(step == pl.num_programs(1) - 1)
    def _():
        out_ref[...] = acc_ref[...].astype(out_ref.dtype)


def pool_spec(width, group, i):
    return pl.BlockSpec(
        (1, BLK, width), lambda s, g, idx, lens: (idx[s * MAXB + g * group + i], 0, 0)
    )


def attention(index, slot_lengths, query_pad, pool, group=8):
    rows, width = query_pad.shape
    slots = rows // CAND
    heads = width // (2 * DH)
    kernel = functools.partial(attention_kernel, heads=heads, group=group)
    grid_spec = pltpu.PrefetchScalarGridSpec(
        num_scalar_prefetch=2,
        grid=(slots, MAXB // group),
        in_specs=[pl.BlockSpec((CAND, width), lambda s, g, idx, lens: (s, 0))]
        + [pool_spec(width, group, i) for i in range(group)],
        out_specs=pl.BlockSpec((CAND, width), lambda s, g, idx, lens: (s, 0)),
        scratch_shapes=[pltpu.VMEM((CAND, width), jnp.float32)],
    )
    return pl.pallas_call(
        kernel,
        grid_spec=grid_spec,
        out_shape=jax.ShapeDtypeStruct((rows, width), jnp.bfloat16),
        compiler_params=pltpu.CompilerParams(dimension_semantics=("arbitrary", "arbitrary")),
    )(index, slot_lengths, query_pad, *([pool] * group))


def shards(tokens, w_proj, w_out, kv_cache, slot_request, lengths, block_owner):
    head_local = w_proj.shape[1] // (2 * DH)
    received = lax.all_to_all(kv_cache, "req", split_axis=1, concat_axis=0, tiled=True)
    most_slots = received.shape[2]
    pool = received.reshape(-1, BLK, received.shape[-1])
    pool_count = pool.shape[0]

    gathered = lax.all_gather(tokens, "head", axis=0, tiled=True)
    normed = layer_norm(gathered.astype(jnp.float32)).astype(jnp.bfloat16)
    row_count = normed.shape[0]
    slots = row_count // CAND
    proj = jax.nn.silu(jnp.dot(normed, w_proj, preferred_element_type=jnp.float32))
    proj = proj.reshape(row_count, head_local, 2, DH)
    gate_u = proj[:, :, 0].astype(jnp.bfloat16).reshape(row_count, head_local * DH)
    query = proj[:, :, 1].astype(jnp.bfloat16)
    query_pad = jnp.concatenate([query, jnp.zeros_like(query)], axis=2).reshape(
        row_count, head_local * 2 * DH
    )

    owner_count = lax.axis_size("req")
    owners = block_owner[:, 0]
    onehot = (owners[:, None] == jnp.arange(owner_count, dtype=jnp.int32)[None, :]).astype(
        jnp.int32
    )
    rank = jnp.sum((jnp.cumsum(onehot, axis=0) - onehot) * onehot, axis=1)
    index = jnp.clip(owners * most_slots + rank, 0, pool_count - 1).reshape(slots, MAXB)
    total_requests = lengths.shape[0]
    match = slot_request[:, None] == jnp.arange(total_requests, dtype=jnp.int32)[None, :]
    slot_lengths = jnp.sum(jnp.where(match, lengths[None, :], 0), axis=1).astype(jnp.int32)
    last_live = jnp.clip((slot_lengths - 1) // BLK, 0, MAXB - 1)
    blocks = jnp.minimum(jnp.arange(MAXB, dtype=jnp.int32)[None, :], last_live[:, None])
    index = jnp.take_along_axis(index, blocks, axis=1).reshape(-1).astype(jnp.int32)

    out = attention(index, slot_lengths, query_pad, pool)
    attn = out.reshape(row_count, head_local, 2, DH)[:, :, 1].reshape(row_count, head_local * DH)

    gate_rows = lax.all_to_all(gate_u, "head", split_axis=0, concat_axis=1, tiled=True)
    attn_rows = lax.all_to_all(attn, "head", split_axis=0, concat_axis=1, tiled=True)
    attn_rows = attn_rows.astype(jnp.float32)
    gate_rows = gate_rows.astype(jnp.float32)
    hidden = (layer_norm(attn_rows) * gate_rows).astype(jnp.bfloat16)
    return jnp.dot(hidden, w_out, preferred_element_type=jnp.float32).astype(jnp.bfloat16)


def solution(mesh):
    return jax.shard_map(
        shards,
        mesh=mesh,
        in_specs=(
            P(("req", "head"), None),
            P(None, "head"),
            P(),
            P("req", None, None, None, "head"),
            P("req"),
            P(),
            P("req", None),
        ),
        out_specs=P(("req", "head"), None),
        check_vma=False,
    )
```

```python
import functools

import jax
import jax.numpy as jnp
from jax import lax
from jax.experimental import pallas as pl
from jax.experimental.pallas import tpu as pltpu
from jax.sharding import PartitionSpec as P

DH = 64
CAND = 512
BLK = 128
MAXB = 32


def layer_norm(values):
    mean = jnp.mean(values, axis=-1, keepdims=True)
    square = jnp.mean(values * values, axis=-1, keepdims=True)
    return (values - mean) * lax.rsqrt(square - mean * mean + 1e-05)


def attention_kernel(index_ref, length_ref, query_ref, *refs, heads, group):
    pool_refs = refs[:group]
    out_ref, acc_ref = refs[group:]
    slot = pl.program_id(0)
    step = pl.program_id(1)
    length = length_ref[slot]

    @pl.when(step == 0)
    def _():
        acc_ref[...] = jnp.zeros_like(acc_ref)

    span = group * BLK

    @pl.when(step * span < length)
    def _():
        kv = jnp.concatenate([ref[0] for ref in pool_refs], axis=0)
        positions = step * span + lax.broadcasted_iota(jnp.int32, (span, 1), 0)
        kv = jnp.where(positions < length, kv, jnp.zeros_like(kv))
        for h in range(heads):
            lanes = slice(h * 2 * DH, (h + 1) * 2 * DH)
            pair = kv[:, lanes]
            query = query_ref[:, lanes]
            half = lax.dot_general(
                query, pair, (((1,), (1,)), ((), ())), preferred_element_type=jnp.float32
            ) * (0.5 / DH**0.5)
            weights = (half + half * jnp.tanh(half)).astype(jnp.bfloat16)
            acc_ref[:, lanes] += jnp.dot(weights, pair, preferred_element_type=jnp.float32)

    @pl.when(step == pl.num_programs(1) - 1)
    def _():
        out_ref[...] = acc_ref[...].astype(out_ref.dtype)


def pool_spec(width, group, i):
    return pl.BlockSpec(
        (1, BLK, width), lambda s, g, idx, lens: (idx[s * MAXB + g * group + i], 0, 0)
    )


def attention(index, slot_lengths, query_pad, pool, group=8):
    rows, width = query_pad.shape
    slots = rows // CAND
    heads = width // (2 * DH)
    kernel = functools.partial(attention_kernel, heads=heads, group=group)
    grid_spec = pltpu.PrefetchScalarGridSpec(
        num_scalar_prefetch=2,
        grid=(slots, MAXB // group),
        in_specs=[pl.BlockSpec((CAND, width), lambda s, g, idx, lens: (s, 0))]
        + [pool_spec(width, group, i) for i in range(group)],
        out_specs=pl.BlockSpec((CAND, width), lambda s, g, idx, lens: (s, 0)),
        scratch_shapes=[pltpu.VMEM((CAND, width), jnp.float32)],
    )
    return pl.pallas_call(
        kernel,
        grid_spec=grid_spec,
        out_shape=jax.ShapeDtypeStruct((rows, width), jnp.bfloat16),
        compiler_params=pltpu.CompilerParams(dimension_semantics=("arbitrary", "arbitrary")),
    )(index, slot_lengths, query_pad, *([pool] * group))


def shards(tokens, w_proj, w_out, kv_cache, slot_request, lengths, block_owner):
    head_local = w_proj.shape[1] // (2 * DH)
    received = lax.all_to_all(kv_cache, "req", split_axis=1, concat_axis=0, tiled=True)
    most_slots = received.shape[2]
    pool = received.reshape(-1, BLK, received.shape[-1])
    pool_count = pool.shape[0]

    gathered = lax.all_gather(tokens, "head", axis=0, tiled=True)
    normed = layer_norm(gathered.astype(jnp.float32)).astype(jnp.bfloat16)
    row_count = normed.shape[0]
    slots = row_count // CAND
    proj = jax.nn.silu(jnp.dot(normed, w_proj, preferred_element_type=jnp.float32))
    proj = proj.reshape(row_count, head_local, 2, DH)
    gate_u = proj[:, :, 0].astype(jnp.bfloat16).reshape(row_count, head_local * DH)
    query = proj[:, :, 1].astype(jnp.bfloat16)
    query_pad = jnp.concatenate([query, jnp.zeros_like(query)], axis=2).reshape(
        row_count, head_local * 2 * DH
    )

    owner_count = lax.axis_size("req")
    owners = block_owner[:, 0]
    onehot = (owners[:, None] == jnp.arange(owner_count, dtype=jnp.int32)[None, :]).astype(
        jnp.int32
    )
    rank = jnp.sum((jnp.cumsum(onehot, axis=0) - onehot) * onehot, axis=1)
    index = jnp.clip(owners * most_slots + rank, 0, pool_count - 1).reshape(slots, MAXB)
    total_requests = lengths.shape[0]
    match = slot_request[:, None] == jnp.arange(total_requests, dtype=jnp.int32)[None, :]
    slot_lengths = jnp.sum(jnp.where(match, lengths[None, :], 0), axis=1).astype(jnp.int32)
    last_live = jnp.clip((slot_lengths - 1) // BLK, 0, MAXB - 1)
    blocks = jnp.minimum(jnp.arange(MAXB, dtype=jnp.int32)[None, :], last_live[:, None])
    index = jnp.take_along_axis(index, blocks, axis=1).reshape(-1).astype(jnp.int32)

    out = attention(index, slot_lengths, query_pad, pool)
    attn = out.reshape(row_count, head_local, 2, DH)[:, :, 1].reshape(row_count, head_local * DH)

    moved = lax.all_to_all(jnp.stack([attn, gate_u]), "head", split_axis=1, concat_axis=2, tiled=True)
    attn_rows = moved[0].astype(jnp.float32)
    gate_rows = moved[1].astype(jnp.float32)
    hidden = (layer_norm(attn_rows) * gate_rows).astype(jnp.bfloat16)
    return jnp.dot(hidden, w_out, preferred_element_type=jnp.float32).astype(jnp.bfloat16)


def solution(mesh):
    return jax.shard_map(
        shards,
        mesh=mesh,
        in_specs=(
            P(("req", "head"), None),
            P(None, "head"),
            P(),
            P("req", None, None, None, "head"),
            P("req"),
            P(),
            P("req", None),
        ),
        out_specs=P(("req", "head"), None),
        check_vma=False,
    )
```

```python
import functools

import jax
import jax.numpy as jnp
from jax import lax
from jax.experimental import pallas as pl
from jax.experimental.pallas import tpu as pltpu
from jax.sharding import PartitionSpec as P

DH = 64
CAND = 512
BLK = 128
MAXB = 32


def layer_norm(values):
    mean = jnp.mean(values, axis=-1, keepdims=True)
    square = jnp.mean(values * values, axis=-1, keepdims=True)
    return (values - mean) * lax.rsqrt(square - mean * mean + 1e-05)


def attention_kernel(index_ref, length_ref, query_ref, *refs, heads, group):
    pool_refs = refs[:group]
    out_ref, acc_ref = refs[group:]
    slot = pl.program_id(0)
    step = pl.program_id(1)
    length = length_ref[slot]

    @pl.when(step == 0)
    def _():
        acc_ref[...] = jnp.zeros_like(acc_ref)

    span = group * BLK

    @pl.when(step * span < length)
    def _():
        kv = jnp.concatenate([ref[0] for ref in pool_refs], axis=0)
        positions = step * span + lax.broadcasted_iota(jnp.int32, (span, 1), 0)
        kv = jnp.where(positions < length, kv, jnp.zeros_like(kv))
        for h in range(heads):
            lanes = slice(h * 2 * DH, (h + 1) * 2 * DH)
            pair = kv[:, lanes]
            query = query_ref[:, lanes]
            half = lax.dot_general(
                query, pair, (((1,), (1,)), ((), ())), preferred_element_type=jnp.float32
            ) * (0.5 / DH**0.5)
            weights = (half + half * jnp.tanh(half)).astype(jnp.bfloat16)
            acc_ref[:, lanes] += jnp.dot(weights, pair, preferred_element_type=jnp.float32)

    @pl.when(step == pl.num_programs(1) - 1)
    def _():
        out_ref[...] = acc_ref[...].astype(out_ref.dtype)


def pool_spec(width, group, i):
    return pl.BlockSpec(
        (1, BLK, width), lambda s, g, idx, lens: (idx[s * MAXB + g * group + i], 0, 0)
    )


def attention(index, slot_lengths, query_pad, pool, group=8):
    rows, width = query_pad.shape
    slots = rows // CAND
    heads = width // (2 * DH)
    kernel = functools.partial(attention_kernel, heads=heads, group=group)
    grid_spec = pltpu.PrefetchScalarGridSpec(
        num_scalar_prefetch=2,
        grid=(slots, MAXB // group),
        in_specs=[pl.BlockSpec((CAND, width), lambda s, g, idx, lens: (s, 0))]
        + [pool_spec(width, group, i) for i in range(group)],
        out_specs=pl.BlockSpec((CAND, width), lambda s, g, idx, lens: (s, 0)),
        scratch_shapes=[pltpu.VMEM((CAND, width), jnp.float32)],
    )
    return pl.pallas_call(
        kernel,
        grid_spec=grid_spec,
        out_shape=jax.ShapeDtypeStruct((rows, width), jnp.bfloat16),
        compiler_params=pltpu.CompilerParams(dimension_semantics=("arbitrary", "arbitrary")),
    )(index, slot_lengths, query_pad, *([pool] * group))


def exchange(values, axis):
    count = lax.axis_size(axis)
    me = lax.axis_index(axis)
    rows = values.shape[0] // count
    blocks = values.reshape(count, rows, values.shape[1])
    received = []
    for shift in range(count):
        piece = lax.dynamic_index_in_dim(blocks, (me + shift) % count, 0, keepdims=False)
        if shift:
            pairs = [(i, (i + shift) % count) for i in range(count)]
            piece = lax.ppermute(piece, axis, perm=pairs)
        received.append(piece)
    stacked = jnp.stack(received)
    sources = (me - jnp.arange(count, dtype=jnp.int32)) % count
    ordered = jnp.take(stacked, sources, axis=0)
    return jnp.transpose(ordered, (1, 0, 2)).reshape(rows, count * values.shape[1])


def shards(tokens, w_proj, w_out, kv_cache, slot_request, lengths, block_owner):
    head_local = w_proj.shape[1] // (2 * DH)
    received = lax.all_to_all(kv_cache, "req", split_axis=1, concat_axis=0, tiled=True)
    most_slots = received.shape[2]
    pool = received.reshape(-1, BLK, received.shape[-1])
    pool_count = pool.shape[0]

    gathered = lax.all_gather(tokens, "head", axis=0, tiled=True)
    normed = layer_norm(gathered.astype(jnp.float32)).astype(jnp.bfloat16)
    row_count = normed.shape[0]
    slots = row_count // CAND
    proj = jax.nn.silu(jnp.dot(normed, w_proj, preferred_element_type=jnp.float32))
    proj = proj.reshape(row_count, head_local, 2, DH)
    gate_u = proj[:, :, 0].astype(jnp.bfloat16).reshape(row_count, head_local * DH)
    query = proj[:, :, 1].astype(jnp.bfloat16)
    query_pad = jnp.concatenate([query, jnp.zeros_like(query)], axis=2).reshape(
        row_count, head_local * 2 * DH
    )

    owner_count = lax.axis_size("req")
    owners = block_owner[:, 0]
    onehot = (owners[:, None] == jnp.arange(owner_count, dtype=jnp.int32)[None, :]).astype(
        jnp.int32
    )
    rank = jnp.sum((jnp.cumsum(onehot, axis=0) - onehot) * onehot, axis=1)
    index = jnp.clip(owners * most_slots + rank, 0, pool_count - 1).reshape(slots, MAXB)
    total_requests = lengths.shape[0]
    match = slot_request[:, None] == jnp.arange(total_requests, dtype=jnp.int32)[None, :]
    slot_lengths = jnp.sum(jnp.where(match, lengths[None, :], 0), axis=1).astype(jnp.int32)
    last_live = jnp.clip((slot_lengths - 1) // BLK, 0, MAXB - 1)
    blocks = jnp.minimum(jnp.arange(MAXB, dtype=jnp.int32)[None, :], last_live[:, None])
    index = jnp.take_along_axis(index, blocks, axis=1).reshape(-1).astype(jnp.int32)

    gate_rows = exchange(gate_u, "head")
    gate_rows, query_pad = lax.optimization_barrier((gate_rows, query_pad))
    out = attention(index, slot_lengths, query_pad, pool)
    attn = out.reshape(row_count, head_local, 2, DH)[:, :, 1].reshape(row_count, head_local * DH)

    attn_rows = exchange(attn, "head").astype(jnp.float32)
    gate_rows = gate_rows.astype(jnp.float32)
    hidden = (layer_norm(attn_rows) * gate_rows).astype(jnp.bfloat16)
    return jnp.dot(hidden, w_out, preferred_element_type=jnp.float32).astype(jnp.bfloat16)


def solution(mesh):
    return jax.shard_map(
        shards,
        mesh=mesh,
        in_specs=(
            P(("req", "head"), None),
            P(None, "head"),
            P(),
            P("req", None, None, None, "head"),
            P("req"),
            P(),
            P("req", None),
        ),
        out_specs=P(("req", "head"), None),
        check_vma=False,
    )
```

```python
import functools

import jax
import jax.numpy as jnp
from jax import lax
from jax.experimental import pallas as pl
from jax.experimental.pallas import tpu as pltpu
from jax.sharding import PartitionSpec as P

DH = 64
CAND = 512
BLK = 128
MAXB = 32


def layer_norm(values):
    mean = jnp.mean(values, axis=-1, keepdims=True)
    square = jnp.mean(values * values, axis=-1, keepdims=True)
    return (values - mean) * lax.rsqrt(square - mean * mean + 1e-05)


def attention_kernel(index_ref, length_ref, query_ref, *refs, heads, group):
    pool_refs = refs[:group]
    out_ref, acc_ref = refs[group:]
    slot = pl.program_id(0)
    step = pl.program_id(1)
    length = length_ref[slot]

    @pl.when(step == 0)
    def _():
        acc_ref[...] = jnp.zeros_like(acc_ref)

    span = group * BLK

    @pl.when(step * span < length)
    def _():
        kv = jnp.concatenate([ref[0] for ref in pool_refs], axis=0)
        positions = step * span + lax.broadcasted_iota(jnp.int32, (span, 1), 0)
        kv = jnp.where(positions < length, kv, jnp.zeros_like(kv))
        for h in range(heads):
            lanes = slice(h * 2 * DH, (h + 1) * 2 * DH)
            pair = kv[:, lanes]
            query = query_ref[:, lanes]
            half = lax.dot_general(
                query, pair, (((1,), (1,)), ((), ())), preferred_element_type=jnp.float32
            ) * (0.5 / DH**0.5)
            weights = (half + half * jnp.tanh(half)).astype(jnp.bfloat16)
            acc_ref[:, lanes] += jnp.dot(weights, pair, preferred_element_type=jnp.float32)

    @pl.when(step == pl.num_programs(1) - 1)
    def _():
        out_ref[...] = acc_ref[...].astype(out_ref.dtype)


def pool_spec(width, group, i):
    return pl.BlockSpec(
        (1, BLK, width), lambda s, g, idx, lens: (idx[s * MAXB + g * group + i], 0, 0)
    )


def attention(index, slot_lengths, query_pad, pool, group=8):
    rows, width = query_pad.shape
    slots = rows // CAND
    heads = width // (2 * DH)
    kernel = functools.partial(attention_kernel, heads=heads, group=group)
    grid_spec = pltpu.PrefetchScalarGridSpec(
        num_scalar_prefetch=2,
        grid=(slots, MAXB // group),
        in_specs=[pl.BlockSpec((CAND, width), lambda s, g, idx, lens: (s, 0))]
        + [pool_spec(width, group, i) for i in range(group)],
        out_specs=pl.BlockSpec((CAND, width), lambda s, g, idx, lens: (s, 0)),
        scratch_shapes=[pltpu.VMEM((CAND, width), jnp.float32)],
    )
    return pl.pallas_call(
        kernel,
        grid_spec=grid_spec,
        out_shape=jax.ShapeDtypeStruct((rows, width), jnp.bfloat16),
        compiler_params=pltpu.CompilerParams(dimension_semantics=("arbitrary", "arbitrary")),
    )(index, slot_lengths, query_pad, *([pool] * group))


def exchange(values, axis, cores=2):
    count = lax.axis_size(axis)
    chips = count // cores
    me = lax.axis_index(axis)
    my_chip = me // cores
    my_core = me % cores
    rows = values.shape[0] // count
    width = values.shape[1]
    blocks = values.reshape(chips, cores, rows, width)
    keep = lax.dynamic_index_in_dim(blocks, my_core, 1, keepdims=False)
    other = lax.dynamic_index_in_dim(blocks, 1 - my_core, 1, keepdims=False)
    swapped = lax.ppermute(other, axis, perm=[(i, i ^ 1) for i in range(count)])
    both = jnp.stack([keep, swapped], axis=1)
    by_source = jnp.take(both, jnp.stack([my_core, 1 - my_core]), axis=1)
    received = []
    for shift in range(chips):
        piece = lax.dynamic_index_in_dim(by_source, (my_chip + shift) % chips, 0, keepdims=False)
        if shift:
            pairs = [
                (c * cores + k, ((c + shift) % chips) * cores + k)
                for c in range(chips)
                for k in range(cores)
            ]
            piece = lax.ppermute(piece, axis, perm=pairs)
        received.append(piece)
    stacked = jnp.stack(received)
    sources = (my_chip - jnp.arange(chips, dtype=jnp.int32)) % chips
    ordered = jnp.take(stacked, sources, axis=0)
    return jnp.transpose(ordered, (2, 0, 1, 3)).reshape(rows, count * width)


def shards(tokens, w_proj, w_out, kv_cache, slot_request, lengths, block_owner):
    head_local = w_proj.shape[1] // (2 * DH)
    received = lax.all_to_all(kv_cache, "req", split_axis=1, concat_axis=0, tiled=True)
    most_slots = received.shape[2]
    pool = received.reshape(-1, BLK, received.shape[-1])
    pool_count = pool.shape[0]

    gathered = lax.all_gather(tokens, "head", axis=0, tiled=True)
    normed = layer_norm(gathered.astype(jnp.float32)).astype(jnp.bfloat16)
    row_count = normed.shape[0]
    slots = row_count // CAND
    proj = jax.nn.silu(jnp.dot(normed, w_proj, preferred_element_type=jnp.float32))
    proj = proj.reshape(row_count, head_local, 2, DH)
    gate_u = proj[:, :, 0].astype(jnp.bfloat16).reshape(row_count, head_local * DH)
    query = proj[:, :, 1].astype(jnp.bfloat16)
    query_pad = jnp.concatenate([query, jnp.zeros_like(query)], axis=2).reshape(
        row_count, head_local * 2 * DH
    )

    owner_count = lax.axis_size("req")
    owners = block_owner[:, 0]
    onehot = (owners[:, None] == jnp.arange(owner_count, dtype=jnp.int32)[None, :]).astype(
        jnp.int32
    )
    rank = jnp.sum((jnp.cumsum(onehot, axis=0) - onehot) * onehot, axis=1)
    index = jnp.clip(owners * most_slots + rank, 0, pool_count - 1).reshape(slots, MAXB)
    total_requests = lengths.shape[0]
    match = slot_request[:, None] == jnp.arange(total_requests, dtype=jnp.int32)[None, :]
    slot_lengths = jnp.sum(jnp.where(match, lengths[None, :], 0), axis=1).astype(jnp.int32)
    last_live = jnp.clip((slot_lengths - 1) // BLK, 0, MAXB - 1)
    blocks = jnp.minimum(jnp.arange(MAXB, dtype=jnp.int32)[None, :], last_live[:, None])
    index = jnp.take_along_axis(index, blocks, axis=1).reshape(-1).astype(jnp.int32)

    gate_rows = exchange(gate_u, "head")
    gate_rows, query_pad = lax.optimization_barrier((gate_rows, query_pad))
    out = attention(index, slot_lengths, query_pad, pool)
    attn = out.reshape(row_count, head_local, 2, DH)[:, :, 1].reshape(row_count, head_local * DH)

    attn_rows = exchange(attn, "head").astype(jnp.float32)
    gate_rows = gate_rows.astype(jnp.float32)
    hidden = (layer_norm(attn_rows) * gate_rows).astype(jnp.bfloat16)
    return jnp.dot(hidden, w_out, preferred_element_type=jnp.float32).astype(jnp.bfloat16)


def solution(mesh):
    return jax.shard_map(
        shards,
        mesh=mesh,
        in_specs=(
            P(("req", "head"), None),
            P(None, "head"),
            P(),
            P("req", None, None, None, "head"),
            P("req"),
            P(),
            P("req", None),
        ),
        out_specs=P(("req", "head"), None),
        check_vma=False,
    )
```

```python
import functools

import jax
import jax.numpy as jnp
from jax import lax
from jax.experimental import pallas as pl
from jax.experimental.pallas import tpu as pltpu
from jax.sharding import PartitionSpec as P

DH = 64
CAND = 512
BLK = 128
MAXB = 32


def layer_norm(values):
    mean = jnp.mean(values, axis=-1, keepdims=True)
    square = jnp.mean(values * values, axis=-1, keepdims=True)
    return (values - mean) * lax.rsqrt(square - mean * mean + 1e-05)


def attention_kernel(index_ref, length_ref, query_ref, *refs, heads, group):
    pool_refs = refs[:group]
    out_ref, acc_ref = refs[group:]
    slot = pl.program_id(0)
    step = pl.program_id(1)
    length = length_ref[slot]

    @pl.when(step == 0)
    def _():
        acc_ref[...] = jnp.zeros_like(acc_ref)

    span = group * BLK

    @pl.when(step * span < length)
    def _():
        kv = jnp.concatenate([ref[0] for ref in pool_refs], axis=0)
        positions = step * span + lax.broadcasted_iota(jnp.int32, (span, 1), 0)
        kv = jnp.where(positions < length, kv, jnp.zeros_like(kv))
        for h in range(heads):
            lanes = slice(h * 2 * DH, (h + 1) * 2 * DH)
            pair = kv[:, lanes]
            query = query_ref[:, lanes]
            half = lax.dot_general(
                query, pair, (((1,), (1,)), ((), ())), preferred_element_type=jnp.float32
            ) * (0.5 / DH**0.5)
            weights = (half + half * jnp.tanh(half)).astype(jnp.bfloat16)
            acc_ref[:, lanes] += jnp.dot(weights, pair, preferred_element_type=jnp.float32)

    @pl.when(step == pl.num_programs(1) - 1)
    def _():
        out_ref[...] = acc_ref[...].astype(out_ref.dtype)


def pool_spec(width, group, i):
    return pl.BlockSpec(
        (1, BLK, width), lambda s, g, idx, lens: (idx[s * MAXB + g * group + i], 0, 0)
    )


def attention(index, slot_lengths, query_pad, pool, group=8):
    rows, width = query_pad.shape
    slots = rows // CAND
    heads = width // (2 * DH)
    kernel = functools.partial(attention_kernel, heads=heads, group=group)
    grid_spec = pltpu.PrefetchScalarGridSpec(
        num_scalar_prefetch=2,
        grid=(slots, MAXB // group),
        in_specs=[pl.BlockSpec((CAND, width), lambda s, g, idx, lens: (s, 0))]
        + [pool_spec(width, group, i) for i in range(group)],
        out_specs=pl.BlockSpec((CAND, width), lambda s, g, idx, lens: (s, 0)),
        scratch_shapes=[pltpu.VMEM((CAND, width), jnp.float32)],
    )
    return pl.pallas_call(
        kernel,
        grid_spec=grid_spec,
        out_shape=jax.ShapeDtypeStruct((rows, width), jnp.bfloat16),
        compiler_params=pltpu.CompilerParams(dimension_semantics=("arbitrary", "arbitrary")),
    )(index, slot_lengths, query_pad, *([pool] * group))


def exchange(values, axis, cores=2):
    count = lax.axis_size(axis)
    chips = count // cores
    me = lax.axis_index(axis)
    my_chip = me // cores
    my_core = me % cores
    rows = values.shape[0] // count
    width = values.shape[1]
    blocks = values.reshape(chips, cores, rows, width)
    keep = lax.dynamic_index_in_dim(blocks, my_core, 1, keepdims=False)
    other = lax.dynamic_index_in_dim(blocks, 1 - my_core, 1, keepdims=False)
    swapped = lax.ppermute(other, axis, perm=[(i, i ^ 1) for i in range(count)])
    both = jnp.stack([keep, swapped], axis=1)
    by_source = jnp.take(both, jnp.stack([my_core, 1 - my_core]), axis=1)
    received = []
    for shift in range(chips):
        piece = lax.dynamic_index_in_dim(by_source, (my_chip + shift) % chips, 0, keepdims=False)
        if shift:
            pairs = [
                (c * cores + k, ((c + shift) % chips) * cores + k)
                for c in range(chips)
                for k in range(cores)
            ]
            piece = lax.ppermute(piece, axis, perm=pairs)
        received.append(piece)
    stacked = jnp.stack(received)
    sources = (my_chip - jnp.arange(chips, dtype=jnp.int32)) % chips
    ordered = jnp.take(stacked, sources, axis=0)
    return jnp.transpose(ordered, (2, 0, 1, 3)).reshape(rows, count * width)


def gather_rows(values, axis, cores=2):
    count = lax.axis_size(axis)
    chips = count // cores
    me = lax.axis_index(axis)
    my_chip = me // cores
    my_core = me % cores
    swapped = lax.ppermute(values, axis, perm=[(i, i ^ 1) for i in range(count)])
    both = jnp.stack([values, swapped])
    pair = jnp.take(both, jnp.stack([my_core, 1 - my_core]), axis=0)
    received = [pair]
    for shift in range(1, chips):
        pairs = [
            (c * cores + k, ((c + shift) % chips) * cores + k)
            for c in range(chips)
            for k in range(cores)
        ]
        received.append(lax.ppermute(pair, axis, perm=pairs))
    stacked = jnp.stack(received)
    sources = (my_chip - jnp.arange(chips, dtype=jnp.int32)) % chips
    ordered = jnp.take(stacked, sources, axis=0)
    return ordered.reshape(count * values.shape[0], values.shape[1])


def shards(tokens, w_proj, w_out, kv_cache, slot_request, lengths, block_owner):
    head_local = w_proj.shape[1] // (2 * DH)
    received = lax.all_to_all(kv_cache, "req", split_axis=1, concat_axis=0, tiled=True)
    most_slots = received.shape[2]
    pool = received.reshape(-1, BLK, received.shape[-1])
    pool_count = pool.shape[0]

    gathered = gather_rows(tokens, "head")
    normed = layer_norm(gathered.astype(jnp.float32)).astype(jnp.bfloat16)
    row_count = normed.shape[0]
    slots = row_count // CAND
    proj = jax.nn.silu(jnp.dot(normed, w_proj, preferred_element_type=jnp.float32))
    proj = proj.reshape(row_count, head_local, 2, DH)
    gate_u = proj[:, :, 0].astype(jnp.bfloat16).reshape(row_count, head_local * DH)
    query = proj[:, :, 1].astype(jnp.bfloat16)
    query_pad = jnp.concatenate([query, jnp.zeros_like(query)], axis=2).reshape(
        row_count, head_local * 2 * DH
    )

    owner_count = lax.axis_size("req")
    owners = block_owner[:, 0]
    onehot = (owners[:, None] == jnp.arange(owner_count, dtype=jnp.int32)[None, :]).astype(
        jnp.int32
    )
    rank = jnp.sum((jnp.cumsum(onehot, axis=0) - onehot) * onehot, axis=1)
    index = jnp.clip(owners * most_slots + rank, 0, pool_count - 1).reshape(slots, MAXB)
    total_requests = lengths.shape[0]
    match = slot_request[:, None] == jnp.arange(total_requests, dtype=jnp.int32)[None, :]
    slot_lengths = jnp.sum(jnp.where(match, lengths[None, :], 0), axis=1).astype(jnp.int32)
    last_live = jnp.clip((slot_lengths - 1) // BLK, 0, MAXB - 1)
    blocks = jnp.minimum(jnp.arange(MAXB, dtype=jnp.int32)[None, :], last_live[:, None])
    index = jnp.take_along_axis(index, blocks, axis=1).reshape(-1).astype(jnp.int32)

    gate_rows = exchange(gate_u, "head")
    gate_rows, query_pad = lax.optimization_barrier((gate_rows, query_pad))
    out = attention(index, slot_lengths, query_pad, pool)
    attn = out.reshape(row_count, head_local, 2, DH)[:, :, 1].reshape(row_count, head_local * DH)

    attn_rows = exchange(attn, "head").astype(jnp.float32)
    gate_rows = gate_rows.astype(jnp.float32)
    hidden = (layer_norm(attn_rows) * gate_rows).astype(jnp.bfloat16)
    return jnp.dot(hidden, w_out, preferred_element_type=jnp.float32).astype(jnp.bfloat16)


def solution(mesh):
    return jax.shard_map(
        shards,
        mesh=mesh,
        in_specs=(
            P(("req", "head"), None),
            P(None, "head"),
            P(),
            P("req", None, None, None, "head"),
            P("req"),
            P(),
            P("req", None),
        ),
        out_specs=P(("req", "head"), None),
        check_vma=False,
    )
```

```python
import functools

import jax
import jax.numpy as jnp
from jax import lax
from jax.experimental import pallas as pl
from jax.experimental.pallas import tpu as pltpu
from jax.sharding import PartitionSpec as P

DH = 64
CAND = 512
BLK = 128
MAXB = 32


def layer_norm(values):
    mean = jnp.mean(values, axis=-1, keepdims=True)
    square = jnp.mean(values * values, axis=-1, keepdims=True)
    return (values - mean) * lax.rsqrt(square - mean * mean + 1e-05)


def attention_kernel(index_ref, length_ref, query_ref, *refs, heads, group):
    pool_refs = refs[:group]
    out_ref, acc_ref = refs[group:]
    slot = pl.program_id(0)
    step = pl.program_id(1)
    length = length_ref[slot]

    @pl.when(step == 0)
    def _():
        acc_ref[...] = jnp.zeros_like(acc_ref)

    span = group * BLK

    @pl.when(step * span < length)
    def _():
        kv = jnp.concatenate([ref[0] for ref in pool_refs], axis=0)
        positions = step * span + lax.broadcasted_iota(jnp.int32, (span, 1), 0)
        kv = jnp.where(positions < length, kv, jnp.zeros_like(kv))
        for h in range(heads):
            lanes = slice(h * 2 * DH, (h + 1) * 2 * DH)
            pair = kv[:, lanes]
            query = query_ref[:, lanes]
            half = lax.dot_general(
                query, pair, (((1,), (1,)), ((), ())), preferred_element_type=jnp.float32
            )
            weights = (half + half * jnp.tanh(half)).astype(jnp.bfloat16)
            acc_ref[:, lanes] += jnp.dot(weights, pair, preferred_element_type=jnp.float32)

    @pl.when(step == pl.num_programs(1) - 1)
    def _():
        out_ref[...] = acc_ref[...].astype(out_ref.dtype)


def pool_spec(width, group, i):
    return pl.BlockSpec(
        (1, BLK, width), lambda s, g, idx, lens: (idx[s * MAXB + g * group + i], 0, 0)
    )


def attention(index, slot_lengths, query_pad, pool, group=16):
    rows, width = query_pad.shape
    slots = rows // CAND
    heads = width // (2 * DH)
    kernel = functools.partial(attention_kernel, heads=heads, group=group)
    grid_spec = pltpu.PrefetchScalarGridSpec(
        num_scalar_prefetch=2,
        grid=(slots, MAXB // group),
        in_specs=[pl.BlockSpec((CAND, width), lambda s, g, idx, lens: (s, 0))]
        + [pool_spec(width, group, i) for i in range(group)],
        out_specs=pl.BlockSpec((CAND, width), lambda s, g, idx, lens: (s, 0)),
        scratch_shapes=[pltpu.VMEM((CAND, width), jnp.float32)],
    )
    return pl.pallas_call(
        kernel,
        grid_spec=grid_spec,
        out_shape=jax.ShapeDtypeStruct((rows, width), jnp.bfloat16),
        compiler_params=pltpu.CompilerParams(dimension_semantics=("arbitrary", "arbitrary")),
    )(index, slot_lengths, query_pad, *([pool] * group))


def exchange(values, axis, cores=2):
    count = lax.axis_size(axis)
    chips = count // cores
    me = lax.axis_index(axis)
    my_chip = me // cores
    my_core = me % cores
    rows = values.shape[0] // count
    width = values.shape[1]
    blocks = values.reshape(chips, cores, rows, width)
    keep = lax.dynamic_index_in_dim(blocks, my_core, 1, keepdims=False)
    other = lax.dynamic_index_in_dim(blocks, 1 - my_core, 1, keepdims=False)
    swapped = lax.ppermute(other, axis, perm=[(i, i ^ 1) for i in range(count)])
    both = jnp.stack([keep, swapped], axis=1)
    by_source = jnp.take(both, jnp.stack([my_core, 1 - my_core]), axis=1)
    received = []
    for shift in range(chips):
        piece = lax.dynamic_index_in_dim(by_source, (my_chip + shift) % chips, 0, keepdims=False)
        if shift:
            pairs = [
                (c * cores + k, ((c + shift) % chips) * cores + k)
                for c in range(chips)
                for k in range(cores)
            ]
            piece = lax.ppermute(piece, axis, perm=pairs)
        received.append(piece)
    stacked = jnp.stack(received)
    sources = (my_chip - jnp.arange(chips, dtype=jnp.int32)) % chips
    ordered = jnp.take(stacked, sources, axis=0)
    return jnp.transpose(ordered, (2, 0, 1, 3)).reshape(rows, count * width)


def gather_rows(values, axis, cores=2):
    count = lax.axis_size(axis)
    chips = count // cores
    me = lax.axis_index(axis)
    my_chip = me // cores
    my_core = me % cores
    swapped = lax.ppermute(values, axis, perm=[(i, i ^ 1) for i in range(count)])
    both = jnp.stack([values, swapped])
    pair = jnp.take(both, jnp.stack([my_core, 1 - my_core]), axis=0)
    received = [pair]
    for shift in range(1, chips):
        pairs = [
            (c * cores + k, ((c + shift) % chips) * cores + k)
            for c in range(chips)
            for k in range(cores)
        ]
        received.append(lax.ppermute(pair, axis, perm=pairs))
    stacked = jnp.stack(received)
    sources = (my_chip - jnp.arange(chips, dtype=jnp.int32)) % chips
    ordered = jnp.take(stacked, sources, axis=0)
    return ordered.reshape(count * values.shape[0], values.shape[1])


def shards(tokens, w_proj, w_out, kv_cache, slot_request, lengths, block_owner):
    head_local = w_proj.shape[1] // (2 * DH)
    received = lax.all_to_all(kv_cache, "req", split_axis=1, concat_axis=0, tiled=True)
    most_slots = received.shape[2]
    pool = received.reshape(-1, BLK, received.shape[-1])
    pool_count = pool.shape[0]

    gathered = gather_rows(tokens, "head")
    normed = layer_norm(gathered.astype(jnp.float32)).astype(jnp.bfloat16)
    row_count = normed.shape[0]
    slots = row_count // CAND
    proj = jax.nn.silu(jnp.dot(normed, w_proj, preferred_element_type=jnp.float32))
    proj = proj.reshape(row_count, head_local, 2, DH)
    gate_u = proj[:, :, 0].astype(jnp.bfloat16).reshape(row_count, head_local * DH)
    query = proj[:, :, 1].astype(jnp.bfloat16) * jnp.bfloat16(0.5 / DH**0.5)
    query_pad = jnp.concatenate([query, jnp.zeros_like(query)], axis=2).reshape(
        row_count, head_local * 2 * DH
    )

    owner_count = lax.axis_size("req")
    owners = block_owner[:, 0]
    onehot = (owners[:, None] == jnp.arange(owner_count, dtype=jnp.int32)[None, :]).astype(
        jnp.int32
    )
    rank = jnp.sum((jnp.cumsum(onehot, axis=0) - onehot) * onehot, axis=1)
    index = jnp.clip(owners * most_slots + rank, 0, pool_count - 1).reshape(slots, MAXB)
    total_requests = lengths.shape[0]
    match = slot_request[:, None] == jnp.arange(total_requests, dtype=jnp.int32)[None, :]
    slot_lengths = jnp.sum(jnp.where(match, lengths[None, :], 0), axis=1).astype(jnp.int32)
    last_live = jnp.clip((slot_lengths - 1) // BLK, 0, MAXB - 1)
    blocks = jnp.minimum(jnp.arange(MAXB, dtype=jnp.int32)[None, :], last_live[:, None])
    index = jnp.take_along_axis(index, blocks, axis=1).reshape(-1).astype(jnp.int32)

    gate_rows = exchange(gate_u, "head")
    gate_rows, query_pad = lax.optimization_barrier((gate_rows, query_pad))
    out = attention(index, slot_lengths, query_pad, pool)
    attn = out.reshape(row_count, head_local, 2, DH)[:, :, 1].reshape(row_count, head_local * DH)

    attn_rows = lax.all_to_all(attn, "head", split_axis=0, concat_axis=1, tiled=True)
    attn_rows = attn_rows.astype(jnp.float32)
    gate_rows = gate_rows.astype(jnp.float32)
    hidden = (layer_norm(attn_rows) * gate_rows).astype(jnp.bfloat16)
    return jnp.dot(hidden, w_out, preferred_element_type=jnp.float32).astype(jnp.bfloat16)


def solution(mesh):
    return jax.shard_map(
        shards,
        mesh=mesh,
        in_specs=(
            P(("req", "head"), None),
            P(None, "head"),
            P(),
            P("req", None, None, None, "head"),
            P("req"),
            P(),
            P("req", None),
        ),
        out_specs=P(("req", "head"), None),
        check_vma=False,
    )
```

```python
import functools

import jax
import jax.numpy as jnp
from jax import lax
from jax.experimental import pallas as pl
from jax.experimental.pallas import tpu as pltpu
from jax.sharding import Mesh, PartitionSpec as P

DH = 64
CAND = 512
BLK = 128
MAXB = 32


def layer_norm(values):
    mean = jnp.mean(values, axis=-1, keepdims=True)
    square = jnp.mean(values * values, axis=-1, keepdims=True)
    return (values - mean) * lax.rsqrt(square - mean * mean + 1e-05)


def attention_kernel(index_ref, length_ref, query_ref, *refs, heads, group):
    pool_refs = refs[:group]
    out_ref, acc_ref = refs[group:]
    slot = pl.program_id(0)
    step = pl.program_id(1)
    length = length_ref[slot]

    @pl.when(step == 0)
    def _():
        acc_ref[...] = jnp.zeros_like(acc_ref)

    span = group * BLK

    @pl.when(step * span < length)
    def _():
        kv = jnp.concatenate([ref[0] for ref in pool_refs], axis=0)
        positions = step * span + lax.broadcasted_iota(jnp.int32, (span, 1), 0)
        kv = jnp.where(positions < length, kv, jnp.zeros_like(kv))
        for h in range(heads):
            lanes = slice(h * 2 * DH, (h + 1) * 2 * DH)
            pair = kv[:, lanes]
            query = query_ref[:, lanes]
            half = lax.dot_general(
                query, pair, (((1,), (1,)), ((), ())), preferred_element_type=jnp.float32
            )
            weights = (half + half * jnp.tanh(half)).astype(jnp.bfloat16)
            acc_ref[:, lanes] += jnp.dot(weights, pair, preferred_element_type=jnp.float32)

    @pl.when(step == pl.num_programs(1) - 1)
    def _():
        out_ref[...] = acc_ref[...].astype(out_ref.dtype)


def pool_spec(width, group, i):
    return pl.BlockSpec(
        (1, BLK, width), lambda s, g, idx, lens: (idx[s * MAXB + g * group + i], 0, 0)
    )


def attention(index, slot_lengths, query_pad, pool, group=16):
    rows, width = query_pad.shape
    slots = rows // CAND
    heads = width // (2 * DH)
    kernel = functools.partial(attention_kernel, heads=heads, group=group)
    grid_spec = pltpu.PrefetchScalarGridSpec(
        num_scalar_prefetch=2,
        grid=(slots, MAXB // group),
        in_specs=[pl.BlockSpec((CAND, width), lambda s, g, idx, lens: (s, 0))]
        + [pool_spec(width, group, i) for i in range(group)],
        out_specs=pl.BlockSpec((CAND, width), lambda s, g, idx, lens: (s, 0)),
        scratch_shapes=[pltpu.VMEM((CAND, width), jnp.float32)],
    )
    return pl.pallas_call(
        kernel,
        grid_spec=grid_spec,
        out_shape=jax.ShapeDtypeStruct((rows, width), jnp.bfloat16),
        compiler_params=pltpu.CompilerParams(dimension_semantics=("arbitrary", "arbitrary")),
    )(index, slot_lengths, query_pad, *([pool] * group))


def exchange(values, chip_axis, core_axis):
    chips = lax.axis_size(chip_axis)
    cores = lax.axis_size(core_axis)
    count = chips * cores
    my_core = lax.axis_index(core_axis)
    rows = values.shape[0] // count
    width = values.shape[1]
    blocks = values.reshape(chips, cores, rows, width)
    keep = lax.dynamic_index_in_dim(blocks, my_core, 1, keepdims=False)
    other = lax.dynamic_index_in_dim(blocks, 1 - my_core, 1, keepdims=False)
    swapped = lax.ppermute(other, (chip_axis, core_axis), perm=[(i, i ^ 1) for i in range(count)])
    both = jnp.stack([keep, swapped], axis=1)
    by_source = jnp.take(both, jnp.stack([my_core, 1 - my_core]), axis=1)
    ordered = lax.all_to_all(by_source, chip_axis, split_axis=0, concat_axis=0, tiled=True)
    return jnp.transpose(ordered, (2, 0, 1, 3)).reshape(rows, count * width)


def exchange_permutes(values, chip_axis, core_axis):
    chips = lax.axis_size(chip_axis)
    cores = lax.axis_size(core_axis)
    count = chips * cores
    axis = (chip_axis, core_axis)
    my_chip = lax.axis_index(chip_axis)
    my_core = lax.axis_index(core_axis)
    rows = values.shape[0] // count
    width = values.shape[1]
    blocks = values.reshape(chips, cores, rows, width)
    keep = lax.dynamic_index_in_dim(blocks, my_core, 1, keepdims=False)
    other = lax.dynamic_index_in_dim(blocks, 1 - my_core, 1, keepdims=False)
    swapped = lax.ppermute(other, axis, perm=[(i, i ^ 1) for i in range(count)])
    both = jnp.stack([keep, swapped], axis=1)
    by_source = jnp.take(both, jnp.stack([my_core, 1 - my_core]), axis=1)
    received = []
    for shift in range(chips):
        piece = lax.dynamic_index_in_dim(by_source, (my_chip + shift) % chips, 0, keepdims=False)
        if shift:
            pairs = [
                (c * cores + k, ((c + shift) % chips) * cores + k)
                for c in range(chips)
                for k in range(cores)
            ]
            piece = lax.ppermute(piece, axis, perm=pairs)
        received.append(piece)
    stacked = jnp.stack(received)
    sources = (my_chip - jnp.arange(chips, dtype=jnp.int32)) % chips
    ordered = jnp.take(stacked, sources, axis=0)
    return jnp.transpose(ordered, (2, 0, 1, 3)).reshape(rows, count * width)


def gather_rows(values, chip_axis, core_axis):
    chips = lax.axis_size(chip_axis)
    cores = lax.axis_size(core_axis)
    count = chips * cores
    axis = (chip_axis, core_axis)
    my_chip = lax.axis_index(chip_axis)
    my_core = lax.axis_index(core_axis)
    swapped = lax.ppermute(values, axis, perm=[(i, i ^ 1) for i in range(count)])
    both = jnp.stack([values, swapped])
    pair = jnp.take(both, jnp.stack([my_core, 1 - my_core]), axis=0)
    received = [pair]
    for shift in range(1, chips):
        pairs = [
            (c * cores + k, ((c + shift) % chips) * cores + k)
            for c in range(chips)
            for k in range(cores)
        ]
        received.append(lax.ppermute(pair, axis, perm=pairs))
    stacked = jnp.stack(received)
    sources = (my_chip - jnp.arange(chips, dtype=jnp.int32)) % chips
    ordered = jnp.take(stacked, sources, axis=0)
    return ordered.reshape(count * values.shape[0], values.shape[1])


def shards(tokens, w_proj, w_out, kv_cache, slot_request, lengths, block_owner):
    head_local = w_proj.shape[1] // (2 * DH)
    received = lax.all_to_all(kv_cache, "req", split_axis=1, concat_axis=0, tiled=True)
    most_slots = received.shape[2]
    pool = received.reshape(-1, BLK, received.shape[-1])
    pool_count = pool.shape[0]

    gathered = gather_rows(tokens, "hx", "hc")
    normed = layer_norm(gathered.astype(jnp.float32)).astype(jnp.bfloat16)
    row_count = normed.shape[0]
    slots = row_count // CAND
    proj = jax.nn.silu(jnp.dot(normed, w_proj, preferred_element_type=jnp.float32))
    proj = proj.reshape(row_count, head_local, 2, DH)
    gate_u = proj[:, :, 0].astype(jnp.bfloat16).reshape(row_count, head_local * DH)
    query = proj[:, :, 1].astype(jnp.bfloat16) * jnp.bfloat16(0.5 / DH**0.5)
    query_pad = jnp.concatenate([query, jnp.zeros_like(query)], axis=2).reshape(
        row_count, head_local * 2 * DH
    )

    owner_count = lax.axis_size("req")
    owners = block_owner[:, 0]
    onehot = (owners[:, None] == jnp.arange(owner_count, dtype=jnp.int32)[None, :]).astype(
        jnp.int32
    )
    rank = jnp.sum((jnp.cumsum(onehot, axis=0) - onehot) * onehot, axis=1)
    index = jnp.clip(owners * most_slots + rank, 0, pool_count - 1).reshape(slots, MAXB)
    total_requests = lengths.shape[0]
    match = slot_request[:, None] == jnp.arange(total_requests, dtype=jnp.int32)[None, :]
    slot_lengths = jnp.sum(jnp.where(match, lengths[None, :], 0), axis=1).astype(jnp.int32)
    last_live = jnp.clip((slot_lengths - 1) // BLK, 0, MAXB - 1)
    blocks = jnp.minimum(jnp.arange(MAXB, dtype=jnp.int32)[None, :], last_live[:, None])
    index = jnp.take_along_axis(index, blocks, axis=1).reshape(-1).astype(jnp.int32)

    gate_rows = exchange_permutes(gate_u, "hx", "hc")
    gate_rows, query_pad = lax.optimization_barrier((gate_rows, query_pad))
    out = attention(index, slot_lengths, query_pad, pool)
    attn = out.reshape(row_count, head_local, 2, DH)[:, :, 1].reshape(row_count, head_local * DH)

    attn_rows = exchange(attn, "hx", "hc")
    attn_rows = attn_rows.astype(jnp.float32)
    gate_rows = gate_rows.astype(jnp.float32)
    hidden = (layer_norm(attn_rows) * gate_rows).astype(jnp.bfloat16)
    return jnp.dot(hidden, w_out, preferred_element_type=jnp.float32).astype(jnp.bfloat16)


def solution(mesh):
    req, head = mesh.devices.shape
    cores = 2
    split = Mesh(mesh.devices.reshape(req, head // cores, cores), ("req", "hx", "hc"))
    heads = ("hx", "hc")
    return jax.shard_map(
        shards,
        mesh=split,
        in_specs=(
            P(("req",) + heads, None),
            P(None, heads),
            P(),
            P("req", None, None, None, heads),
            P("req"),
            P(),
            P("req", None),
        ),
        out_specs=P(("req",) + heads, None),
        check_vma=False,
    )
```

```python
import functools

import jax
import jax.numpy as jnp
from jax import lax
from jax.experimental import pallas as pl
from jax.experimental.pallas import tpu as pltpu
from jax.sharding import PartitionSpec as P

DH = 64
CAND = 512
BLK = 128
MAXB = 32


def layer_norm(values):
    mean = jnp.mean(values, axis=-1, keepdims=True)
    square = jnp.mean(values * values, axis=-1, keepdims=True)
    return (values - mean) * lax.rsqrt(square - mean * mean + 1e-05)


def attention_kernel(index_ref, length_ref, query_ref, *refs, heads, group):
    pool_refs = refs[:group]
    out_ref, acc_ref = refs[group:]
    slot = pl.program_id(0)
    step = pl.program_id(1)
    length = length_ref[slot]

    @pl.when(step == 0)
    def _():
        acc_ref[...] = jnp.zeros_like(acc_ref)

    span = group * BLK

    @pl.when(step * span < length)
    def _():
        kv = jnp.concatenate([ref[0] for ref in pool_refs], axis=0)
        positions = step * span + lax.broadcasted_iota(jnp.int32, (span, 1), 0)
        kv = jnp.where(positions < length, kv, jnp.zeros_like(kv))
        for h in range(heads):
            lanes = slice(h * 2 * DH, (h + 1) * 2 * DH)
            pair = kv[:, lanes]
            query = query_ref[:, lanes]
            half = lax.dot_general(
                query, pair, (((1,), (1,)), ((), ())), preferred_element_type=jnp.float32
            )
            weights = (half + half * jnp.tanh(half)).astype(jnp.bfloat16)
            acc_ref[:, lanes] += jnp.dot(weights, pair, preferred_element_type=jnp.float32)

    @pl.when(step == pl.num_programs(1) - 1)
    def _():
        for q in range(CAND // BLK):
            rows = slice(q * BLK, (q + 1) * BLK)
            values = jnp.concatenate(
                [acc_ref[rows, h * 2 * DH + DH : (h + 1) * 2 * DH] for h in range(heads)], axis=1
            )
            out_ref[q] = values.T.astype(out_ref.dtype)


def pool_spec(width, group, i):
    return pl.BlockSpec(
        (1, BLK, width), lambda s, g, idx, lens: (idx[s * MAXB + g * group + i], 0, 0)
    )


def attention(index, slot_lengths, query_pad, pool, group=16):
    rows, width = query_pad.shape
    slots = rows // CAND
    heads = width // (2 * DH)
    kernel = functools.partial(attention_kernel, heads=heads, group=group)
    grid_spec = pltpu.PrefetchScalarGridSpec(
        num_scalar_prefetch=2,
        grid=(slots, MAXB // group),
        in_specs=[pl.BlockSpec((CAND, width), lambda s, g, idx, lens: (s, 0))]
        + [pool_spec(width, group, i) for i in range(group)],
        out_specs=pl.BlockSpec(
            (CAND // BLK, heads * DH, BLK), lambda s, g, idx, lens: (s, 0, 0)
        ),
        scratch_shapes=[pltpu.VMEM((CAND, width), jnp.float32)],
    )
    return pl.pallas_call(
        kernel,
        grid_spec=grid_spec,
        out_shape=jax.ShapeDtypeStruct((rows // BLK, heads * DH, BLK), jnp.bfloat16),
        compiler_params=pltpu.CompilerParams(dimension_semantics=("arbitrary", "arbitrary")),
    )(index, slot_lengths, query_pad, *([pool] * group))


def exchange(values, axis, cores=2):
    count = lax.axis_size(axis)
    chips = count // cores
    me = lax.axis_index(axis)
    my_chip = me // cores
    my_core = me % cores
    rows = values.shape[0] // count
    width = values.shape[1]
    blocks = values.reshape(chips, cores, rows, width)
    keep = lax.dynamic_index_in_dim(blocks, my_core, 1, keepdims=False)
    other = lax.dynamic_index_in_dim(blocks, 1 - my_core, 1, keepdims=False)
    swapped = lax.ppermute(other, axis, perm=[(i, i ^ 1) for i in range(count)])
    both = jnp.stack([keep, swapped], axis=1)
    by_source = jnp.take(both, jnp.stack([my_core, 1 - my_core]), axis=1)
    received = []
    for shift in range(chips):
        piece = lax.dynamic_index_in_dim(by_source, (my_chip + shift) % chips, 0, keepdims=False)
        if shift:
            pairs = [
                (c * cores + k, ((c + shift) % chips) * cores + k)
                for c in range(chips)
                for k in range(cores)
            ]
            piece = lax.ppermute(piece, axis, perm=pairs)
        received.append(piece)
    stacked = jnp.stack(received)
    sources = (my_chip - jnp.arange(chips, dtype=jnp.int32)) % chips
    ordered = jnp.take(stacked, sources, axis=0)
    return jnp.transpose(ordered, (2, 0, 1, 3)).reshape(rows, count * width)


def gather_rows(values, axis, cores=2):
    count = lax.axis_size(axis)
    chips = count // cores
    me = lax.axis_index(axis)
    my_chip = me // cores
    my_core = me % cores
    swapped = lax.ppermute(values, axis, perm=[(i, i ^ 1) for i in range(count)])
    both = jnp.stack([values, swapped])
    pair = jnp.take(both, jnp.stack([my_core, 1 - my_core]), axis=0)
    received = [pair]
    for shift in range(1, chips):
        pairs = [
            (c * cores + k, ((c + shift) % chips) * cores + k)
            for c in range(chips)
            for k in range(cores)
        ]
        received.append(lax.ppermute(pair, axis, perm=pairs))
    stacked = jnp.stack(received)
    sources = (my_chip - jnp.arange(chips, dtype=jnp.int32)) % chips
    ordered = jnp.take(stacked, sources, axis=0)
    return ordered.reshape(count * values.shape[0], values.shape[1])


def shards(tokens, w_proj, w_out, kv_cache, slot_request, lengths, block_owner):
    head_local = w_proj.shape[1] // (2 * DH)
    received = lax.all_to_all(kv_cache, "req", split_axis=1, concat_axis=0, tiled=True)
    most_slots = received.shape[2]
    pool = received.reshape(-1, BLK, received.shape[-1])
    pool_count = pool.shape[0]

    gathered = gather_rows(tokens, "head")
    normed = layer_norm(gathered.astype(jnp.float32)).astype(jnp.bfloat16)
    row_count = normed.shape[0]
    slots = row_count // CAND
    proj = jax.nn.silu(jnp.dot(normed, w_proj, preferred_element_type=jnp.float32))
    proj = proj.reshape(row_count, head_local, 2, DH)
    gate_u = proj[:, :, 0].astype(jnp.bfloat16).reshape(row_count, head_local * DH)
    query = proj[:, :, 1].astype(jnp.bfloat16) * jnp.bfloat16(0.5 / DH**0.5)
    query_pad = jnp.concatenate([query, jnp.zeros_like(query)], axis=2).reshape(
        row_count, head_local * 2 * DH
    )

    owner_count = lax.axis_size("req")
    owners = block_owner[:, 0]
    onehot = (owners[:, None] == jnp.arange(owner_count, dtype=jnp.int32)[None, :]).astype(
        jnp.int32
    )
    rank = jnp.sum((jnp.cumsum(onehot, axis=0) - onehot) * onehot, axis=1)
    index = jnp.clip(owners * most_slots + rank, 0, pool_count - 1).reshape(slots, MAXB)
    total_requests = lengths.shape[0]
    match = slot_request[:, None] == jnp.arange(total_requests, dtype=jnp.int32)[None, :]
    slot_lengths = jnp.sum(jnp.where(match, lengths[None, :], 0), axis=1).astype(jnp.int32)
    last_live = jnp.clip((slot_lengths - 1) // BLK, 0, MAXB - 1)
    blocks = jnp.minimum(jnp.arange(MAXB, dtype=jnp.int32)[None, :], last_live[:, None])
    index = jnp.take_along_axis(index, blocks, axis=1).reshape(-1).astype(jnp.int32)

    gate_rows = exchange(gate_u, "head")
    gate_rows, query_pad = lax.optimization_barrier((gate_rows, query_pad))
    out = attention(index, slot_lengths, query_pad, pool)
    attn = out.transpose(0, 2, 1).reshape(row_count, head_local * DH)

    attn_rows = lax.all_to_all(attn, "head", split_axis=0, concat_axis=1, tiled=True)
    attn_rows = attn_rows.astype(jnp.float32)
    gate_rows = gate_rows.astype(jnp.float32)
    hidden = (layer_norm(attn_rows) * gate_rows).astype(jnp.bfloat16)
    return jnp.dot(hidden, w_out, preferred_element_type=jnp.float32).astype(jnp.bfloat16)


def solution(mesh):
    return jax.shard_map(
        shards,
        mesh=mesh,
        in_specs=(
            P(("req", "head"), None),
            P(None, "head"),
            P(),
            P("req", None, None, None, "head"),
            P("req"),
            P(),
            P("req", None),
        ),
        out_specs=P(("req", "head"), None),
        check_vma=False,
    )
```

```python
import functools

import jax
import jax.numpy as jnp
from jax import lax
from jax.experimental import pallas as pl
from jax.experimental.pallas import tpu as pltpu
from jax.sharding import PartitionSpec as P

DH = 64
CAND = 512
BLK = 128
MAXB = 32


def layer_norm(values):
    mean = jnp.mean(values, axis=-1, keepdims=True)
    square = jnp.mean(values * values, axis=-1, keepdims=True)
    return (values - mean) * lax.rsqrt(square - mean * mean + 1e-05)


def attention_kernel(index_ref, length_ref, query_ref, *refs, heads, group):
    pool_refs = refs[:group]
    out_ref, acc_ref = refs[group:]
    slot = pl.program_id(0)
    step = pl.program_id(1)
    length = length_ref[slot]

    @pl.when(step == 0)
    def _():
        acc_ref[...] = jnp.zeros_like(acc_ref)

    span = group * BLK

    @pl.when(step * span < length)
    def _():
        kv = jnp.concatenate([ref[0] for ref in pool_refs], axis=0)
        positions = step * span + lax.broadcasted_iota(jnp.int32, (span, 1), 0)
        kv = jnp.where(positions < length, kv, jnp.zeros_like(kv))
        for h in range(heads):
            lanes = slice(h * 2 * DH, (h + 1) * 2 * DH)
            pair = kv[:, lanes]
            query = query_ref[:, lanes]
            half = lax.dot_general(
                query, pair, (((1,), (1,)), ((), ())), preferred_element_type=jnp.float32
            )
            weights = (half + half * jnp.tanh(half)).astype(jnp.bfloat16)
            acc_ref[:, lanes] += jnp.dot(weights, pair, preferred_element_type=jnp.float32)

    @pl.when(step == pl.num_programs(1) - 1)
    def _():
        for q in range(CAND // BLK):
            rows = slice(q * BLK, (q + 1) * BLK)
            values = jnp.concatenate(
                [acc_ref[rows, h * 2 * DH + DH : (h + 1) * 2 * DH] for h in range(heads)], axis=1
            )
            out_ref[q] = values.T.astype(out_ref.dtype)


def pool_spec(width, group, i):
    return pl.BlockSpec(
        (1, BLK, width), lambda s, g, idx, lens: (idx[s * MAXB + g * group + i], 0, 0)
    )


def attention(index, slot_lengths, query_pad, pool, group=32):
    rows, width = query_pad.shape
    slots = rows // CAND
    heads = width // (2 * DH)
    kernel = functools.partial(attention_kernel, heads=heads, group=group)
    grid_spec = pltpu.PrefetchScalarGridSpec(
        num_scalar_prefetch=2,
        grid=(slots, MAXB // group),
        in_specs=[pl.BlockSpec((CAND, width), lambda s, g, idx, lens: (s, 0))]
        + [pool_spec(width, group, i) for i in range(group)],
        out_specs=pl.BlockSpec(
            (CAND // BLK, heads * DH, BLK), lambda s, g, idx, lens: (s, 0, 0)
        ),
        scratch_shapes=[pltpu.VMEM((CAND, width), jnp.float32)],
    )
    return pl.pallas_call(
        kernel,
        grid_spec=grid_spec,
        out_shape=jax.ShapeDtypeStruct((rows // BLK, heads * DH, BLK), jnp.bfloat16),
        compiler_params=pltpu.CompilerParams(dimension_semantics=("arbitrary", "arbitrary")),
    )(index, slot_lengths, query_pad, *([pool] * group))


def exchange(values, axis, cores=2):
    count = lax.axis_size(axis)
    chips = count // cores
    me = lax.axis_index(axis)
    my_chip = me // cores
    my_core = me % cores
    rows = values.shape[0] // count
    width = values.shape[1]
    blocks = values.reshape(chips, cores, rows, width)
    keep = lax.dynamic_index_in_dim(blocks, my_core, 1, keepdims=False)
    other = lax.dynamic_index_in_dim(blocks, 1 - my_core, 1, keepdims=False)
    swapped = lax.ppermute(other, axis, perm=[(i, i ^ 1) for i in range(count)])
    both = jnp.stack([keep, swapped], axis=1)
    by_source = jnp.take(both, jnp.stack([my_core, 1 - my_core]), axis=1)
    received = []
    for shift in range(chips):
        piece = lax.dynamic_index_in_dim(by_source, (my_chip + shift) % chips, 0, keepdims=False)
        if shift:
            pairs = [
                (c * cores + k, ((c + shift) % chips) * cores + k)
                for c in range(chips)
                for k in range(cores)
            ]
            piece = lax.ppermute(piece, axis, perm=pairs)
        received.append(piece)
    stacked = jnp.stack(received)
    sources = (my_chip - jnp.arange(chips, dtype=jnp.int32)) % chips
    ordered = jnp.take(stacked, sources, axis=0)
    return jnp.transpose(ordered, (2, 0, 1, 3)).reshape(rows, count * width)


def gather_rows(values, axis, cores=2):
    count = lax.axis_size(axis)
    chips = count // cores
    me = lax.axis_index(axis)
    my_chip = me // cores
    my_core = me % cores
    swapped = lax.ppermute(values, axis, perm=[(i, i ^ 1) for i in range(count)])
    both = jnp.stack([values, swapped])
    pair = jnp.take(both, jnp.stack([my_core, 1 - my_core]), axis=0)
    received = [pair]
    for shift in range(1, chips):
        pairs = [
            (c * cores + k, ((c + shift) % chips) * cores + k)
            for c in range(chips)
            for k in range(cores)
        ]
        received.append(lax.ppermute(pair, axis, perm=pairs))
    stacked = jnp.stack(received)
    sources = (my_chip - jnp.arange(chips, dtype=jnp.int32)) % chips
    ordered = jnp.take(stacked, sources, axis=0)
    return ordered.reshape(count * values.shape[0], values.shape[1])


def shards(tokens, w_proj, w_out, kv_cache, slot_request, lengths, block_owner):
    head_local = w_proj.shape[1] // (2 * DH)
    received = lax.all_to_all(kv_cache, "req", split_axis=1, concat_axis=0, tiled=True)
    most_slots = received.shape[2]
    pool = received.reshape(-1, BLK, received.shape[-1])
    pool_count = pool.shape[0]

    gathered = gather_rows(tokens, "head")
    normed = layer_norm(gathered.astype(jnp.float32)).astype(jnp.bfloat16)
    row_count = normed.shape[0]
    slots = row_count // CAND
    proj = jax.nn.silu(jnp.dot(normed, w_proj, preferred_element_type=jnp.float32))
    proj = proj.reshape(row_count, head_local, 2, DH)
    gate_u = proj[:, :, 0].astype(jnp.bfloat16).reshape(row_count, head_local * DH)
    query = proj[:, :, 1].astype(jnp.bfloat16) * jnp.bfloat16(0.5 / DH**0.5)
    query_pad = jnp.concatenate([query, jnp.zeros_like(query)], axis=2).reshape(
        row_count, head_local * 2 * DH
    )

    owner_count = lax.axis_size("req")
    owners = block_owner[:, 0]
    onehot = (owners[:, None] == jnp.arange(owner_count, dtype=jnp.int32)[None, :]).astype(
        jnp.int32
    )
    rank = jnp.sum((jnp.cumsum(onehot, axis=0) - onehot) * onehot, axis=1)
    index = jnp.clip(owners * most_slots + rank, 0, pool_count - 1).reshape(slots, MAXB)
    total_requests = lengths.shape[0]
    match = slot_request[:, None] == jnp.arange(total_requests, dtype=jnp.int32)[None, :]
    slot_lengths = jnp.sum(jnp.where(match, lengths[None, :], 0), axis=1).astype(jnp.int32)
    last_live = jnp.clip((slot_lengths - 1) // BLK, 0, MAXB - 1)
    blocks = jnp.minimum(jnp.arange(MAXB, dtype=jnp.int32)[None, :], last_live[:, None])
    index = jnp.take_along_axis(index, blocks, axis=1).reshape(-1).astype(jnp.int32)

    gate_rows = exchange(gate_u, "head")
    gate_rows, query_pad = lax.optimization_barrier((gate_rows, query_pad))
    out = attention(index, slot_lengths, query_pad, pool)
    attn = out.transpose(0, 2, 1).reshape(row_count, head_local * DH)

    attn_rows = lax.all_to_all(attn, "head", split_axis=0, concat_axis=1, tiled=True)
    attn_rows = attn_rows.astype(jnp.float32)
    gate_rows = gate_rows.astype(jnp.float32)
    hidden = (layer_norm(attn_rows) * gate_rows).astype(jnp.bfloat16)
    return jnp.dot(hidden, w_out, preferred_element_type=jnp.float32).astype(jnp.bfloat16)


def solution(mesh):
    return jax.shard_map(
        shards,
        mesh=mesh,
        in_specs=(
            P(("req", "head"), None),
            P(None, "head"),
            P(),
            P("req", None, None, None, "head"),
            P("req"),
            P(),
            P("req", None),
        ),
        out_specs=P(("req", "head"), None),
        check_vma=False,
    )
```

```python
import functools

import jax
import jax.numpy as jnp
from jax import lax
from jax.experimental import pallas as pl
from jax.experimental.pallas import tpu as pltpu
from jax.sharding import PartitionSpec as P

DH = 64
CAND = 512
BLK = 128
MAXB = 32


def layer_norm(values):
    mean = jnp.mean(values, axis=-1, keepdims=True)
    square = jnp.mean(values * values, axis=-1, keepdims=True)
    return (values - mean) * lax.rsqrt(square - mean * mean + 1e-05)


def attention_kernel(index_ref, length_ref, query_ref, *refs, heads, group):
    pool_refs = refs[:group]
    out_ref, acc_ref = refs[group:]
    slot = pl.program_id(0)
    step = pl.program_id(1)
    length = length_ref[slot]

    @pl.when(step == 0)
    def _():
        acc_ref[...] = jnp.zeros_like(acc_ref)

    span = group * BLK

    def accumulate(kv):
        for h in range(heads):
            lanes = slice(h * 2 * DH, (h + 1) * 2 * DH)
            pair = kv[:, lanes]
            query = query_ref[:, lanes]
            half = lax.dot_general(
                query, pair, (((1,), (1,)), ((), ())), preferred_element_type=jnp.float32
            )
            weights = (half + half * jnp.tanh(half)).astype(jnp.bfloat16)
            acc_ref[:, lanes] += jnp.dot(weights, pair, preferred_element_type=jnp.float32)

    @pl.when((step + 1) * span <= length)
    def _():
        accumulate(jnp.concatenate([ref[0] for ref in pool_refs], axis=0))

    @pl.when(jnp.logical_and(step * span < length, length < (step + 1) * span))
    def _():
        kv = jnp.concatenate([ref[0] for ref in pool_refs], axis=0)
        positions = step * span + lax.broadcasted_iota(jnp.int32, (span, 1), 0)
        accumulate(jnp.where(positions < length, kv, jnp.zeros_like(kv)))

    @pl.when(step == pl.num_programs(1) - 1)
    def _():
        for q in range(CAND // BLK):
            rows = slice(q * BLK, (q + 1) * BLK)
            values = jnp.concatenate(
                [acc_ref[rows, h * 2 * DH + DH : (h + 1) * 2 * DH] for h in range(heads)], axis=1
            )
            out_ref[q] = values.T.astype(out_ref.dtype)


def pool_spec(width, group, i):
    return pl.BlockSpec(
        (1, BLK, width), lambda s, g, idx, lens: (idx[s * MAXB + g * group + i], 0, 0)
    )


def attention(index, slot_lengths, query_pad, pool, group=16):
    rows, width = query_pad.shape
    slots = rows // CAND
    heads = width // (2 * DH)
    kernel = functools.partial(attention_kernel, heads=heads, group=group)
    grid_spec = pltpu.PrefetchScalarGridSpec(
        num_scalar_prefetch=2,
        grid=(slots, MAXB // group),
        in_specs=[pl.BlockSpec((CAND, width), lambda s, g, idx, lens: (s, 0))]
        + [pool_spec(width, group, i) for i in range(group)],
        out_specs=pl.BlockSpec(
            (CAND // BLK, heads * DH, BLK), lambda s, g, idx, lens: (s, 0, 0)
        ),
        scratch_shapes=[pltpu.VMEM((CAND, width), jnp.float32)],
    )
    return pl.pallas_call(
        kernel,
        grid_spec=grid_spec,
        out_shape=jax.ShapeDtypeStruct((rows // BLK, heads * DH, BLK), jnp.bfloat16),
        compiler_params=pltpu.CompilerParams(dimension_semantics=("arbitrary", "arbitrary")),
    )(index, slot_lengths, query_pad, *([pool] * group))


def exchange(values, axis, cores=2):
    count = lax.axis_size(axis)
    chips = count // cores
    me = lax.axis_index(axis)
    my_chip = me // cores
    my_core = me % cores
    rows = values.shape[0] // count
    width = values.shape[1]
    blocks = values.reshape(chips, cores, rows, width)
    keep = lax.dynamic_index_in_dim(blocks, my_core, 1, keepdims=False)
    other = lax.dynamic_index_in_dim(blocks, 1 - my_core, 1, keepdims=False)
    swapped = lax.ppermute(other, axis, perm=[(i, i ^ 1) for i in range(count)])
    both = jnp.stack([keep, swapped], axis=1)
    by_source = jnp.take(both, jnp.stack([my_core, 1 - my_core]), axis=1)
    received = []
    for shift in range(chips):
        piece = lax.dynamic_index_in_dim(by_source, (my_chip + shift) % chips, 0, keepdims=False)
        if shift:
            pairs = [
                (c * cores + k, ((c + shift) % chips) * cores + k)
                for c in range(chips)
                for k in range(cores)
            ]
            piece = lax.ppermute(piece, axis, perm=pairs)
        received.append(piece)
    stacked = jnp.stack(received)
    sources = (my_chip - jnp.arange(chips, dtype=jnp.int32)) % chips
    ordered = jnp.take(stacked, sources, axis=0)
    return jnp.transpose(ordered, (2, 0, 1, 3)).reshape(rows, count * width)


def gather_rows(values, axis, cores=2):
    count = lax.axis_size(axis)
    chips = count // cores
    me = lax.axis_index(axis)
    my_chip = me // cores
    my_core = me % cores
    swapped = lax.ppermute(values, axis, perm=[(i, i ^ 1) for i in range(count)])
    both = jnp.stack([values, swapped])
    pair = jnp.take(both, jnp.stack([my_core, 1 - my_core]), axis=0)
    received = [pair]
    for shift in range(1, chips):
        pairs = [
            (c * cores + k, ((c + shift) % chips) * cores + k)
            for c in range(chips)
            for k in range(cores)
        ]
        received.append(lax.ppermute(pair, axis, perm=pairs))
    stacked = jnp.stack(received)
    sources = (my_chip - jnp.arange(chips, dtype=jnp.int32)) % chips
    ordered = jnp.take(stacked, sources, axis=0)
    return ordered.reshape(count * values.shape[0], values.shape[1])


def shards(tokens, w_proj, w_out, kv_cache, slot_request, lengths, block_owner):
    head_local = w_proj.shape[1] // (2 * DH)
    received = lax.all_to_all(kv_cache, "req", split_axis=1, concat_axis=0, tiled=True)
    most_slots = received.shape[2]
    pool = received.reshape(-1, BLK, received.shape[-1])
    pool_count = pool.shape[0]

    gathered = gather_rows(tokens, "head")
    normed = layer_norm(gathered.astype(jnp.float32)).astype(jnp.bfloat16)
    row_count = normed.shape[0]
    slots = row_count // CAND
    proj = jax.nn.silu(jnp.dot(normed, w_proj, preferred_element_type=jnp.float32))
    proj = proj.reshape(row_count, head_local, 2, DH)
    gate_u = proj[:, :, 0].astype(jnp.bfloat16).reshape(row_count, head_local * DH)
    query = proj[:, :, 1].astype(jnp.bfloat16) * jnp.bfloat16(0.5 / DH**0.5)
    query_pad = jnp.concatenate([query, jnp.zeros_like(query)], axis=2).reshape(
        row_count, head_local * 2 * DH
    )

    owner_count = lax.axis_size("req")
    owners = block_owner[:, 0]
    onehot = (owners[:, None] == jnp.arange(owner_count, dtype=jnp.int32)[None, :]).astype(
        jnp.int32
    )
    rank = jnp.sum((jnp.cumsum(onehot, axis=0) - onehot) * onehot, axis=1)
    index = jnp.clip(owners * most_slots + rank, 0, pool_count - 1).reshape(slots, MAXB)
    total_requests = lengths.shape[0]
    match = slot_request[:, None] == jnp.arange(total_requests, dtype=jnp.int32)[None, :]
    slot_lengths = jnp.sum(jnp.where(match, lengths[None, :], 0), axis=1).astype(jnp.int32)
    last_live = jnp.clip((slot_lengths - 1) // BLK, 0, MAXB - 1)
    blocks = jnp.minimum(jnp.arange(MAXB, dtype=jnp.int32)[None, :], last_live[:, None])
    index = jnp.take_along_axis(index, blocks, axis=1).reshape(-1).astype(jnp.int32)

    gate_rows = exchange(gate_u, "head")
    gate_rows, query_pad = lax.optimization_barrier((gate_rows, query_pad))
    out = attention(index, slot_lengths, query_pad, pool)
    attn = out.transpose(0, 2, 1).reshape(row_count, head_local * DH)

    attn_rows = lax.all_to_all(attn, "head", split_axis=0, concat_axis=1, tiled=True)
    attn_rows = attn_rows.astype(jnp.float32)
    gate_rows = gate_rows.astype(jnp.float32)
    hidden = (layer_norm(attn_rows) * gate_rows).astype(jnp.bfloat16)
    return jnp.dot(hidden, w_out, preferred_element_type=jnp.float32).astype(jnp.bfloat16)


def solution(mesh):
    return jax.shard_map(
        shards,
        mesh=mesh,
        in_specs=(
            P(("req", "head"), None),
            P(None, "head"),
            P(),
            P("req", None, None, None, "head"),
            P("req"),
            P(),
            P("req", None),
        ),
        out_specs=P(("req", "head"), None),
        check_vma=False,
    )
```
